256 devices in a mesh: segment: 4 (over y), ctx: 32 (over x_hi, z, core), tp: 2 (over x_lo).
Axes of the slice: x: 4 (x_hi: 2, x_lo: 2; x = x_hi * 2 + x_lo), y: 4, z: 8, core: 2. Of those that a mesh axis runs over, the one named last changes fastest.
Arguments:
- held: bfloat16 [4, 8192, 3584], P('segment', 'ctx'), may hold values from -6 to 6
- text: bfloat16 [8192, 3584], P('ctx'), may hold values from -6 to 6
- frames: bfloat16 [4096, 1024], P('ctx'), may hold values from -6 to 6
- join: int32 [64], P('ctx'), may hold values from 0 to 8128, as said below
- ln_gain: float32 [1024], replicated, may hold values from 0.1 to 1.9
- w_proj: bfloat16 [1024, 3584], P('tp'), may hold values from -0.1875 to 0.1875
- b_proj: float32 [3584], replicated, may hold values from -3 to 3
- norm_gain: float32 [3, 3584], replicated, may hold values from 0.1 to 1.9
- w_qkv: bfloat16 [3, 3584, 2304], P(None, 'ctx', 'tp'), may hold values from -0.09375 to 0.09375
- b_qkv: float32 [3, 2304], P(None, 'tp'), may hold values from -4 to 4
- w_out: bfloat16 [3, 1792, 3584], P(None, 'tp', 'ctx'), may hold values from -1.5 to 1.5
Outputs:
- segment_out: bfloat16 [4, 8192, 3584], P('segment', 'ctx')
The draws below stay inside these ranges and needn't reach their ends.
Inputs may be any that keep to these rules, and one draw needn't show every extreme that they name: `join`: frames never intersect; the 2 frames f with f // 2 == d lie in order inside positions d * 256 to (d + 1) * 256 - 1.
All inputs are finite; a program needn't handle non-finite values.
Results may differ from the reference program's by a relative error of at most 0.015.
Values may be sent and summed in bfloat16 or wider, within the bound.
No kernel may reach another device: no remote copies, remote signals or barrier semaphores. Data moves between devices by JAX's collectives and lax.ppermute only.
A program may use at most 128 MiB of HBM per device.

```python
import math
import jax
import jax.numpy as jnp
from jax import lax

D = 3584
HD = 128
KVH = 2
GROUP = 7
VD = 1024
FRAME = 64
FR_DEV = 2
TOK_DEV = 256
QH = 14
QKV = 2304
LAYERS = 3
TOKENS = 8192
FRAMES = 64
VIS = 4096
N_SEGMENT = 4


def draw_join(key, part):
    devices = FRAMES // FR_DEV
    spare = TOK_DEV - FR_DEV * FRAME
    cuts = jax.random.randint(key, (devices, FR_DEV), 0, spare + 1).astype(jnp.int32)
    cuts = jnp.sort(cuts, axis=1)
    device_ids = jnp.arange(devices, dtype=jnp.int32)[:, None]
    cuts = jnp.where(device_ids == 0, 0, jnp.where(device_ids == devices - 1, spare, cuts))
    starts = device_ids * TOK_DEV + cuts + jnp.arange(FR_DEV, dtype=jnp.int32)[None, :] * FRAME
    return starts.reshape(-1).astype(jnp.int32)


def draw_b_qkv(key, part):
    base = jnp.clip(0.5 * jax.random.normal(key, (LAYERS, KVH, GROUP + 2, HD), jnp.float32), -3.0, 3.0)
    return base.reshape(LAYERS, QKV).astype(jnp.float32)


def levels(key, shape, cuts, least, high):
    loudness = 1.0
    for dim, parts in cuts:
        steps = jax.random.uniform(jax.random.fold_in(jax.random.fold_in(key, 6), dim), (parts,), jnp.float32, least / len(cuts), high / len(cuts))
        loudness = loudness * jnp.repeat(jnp.exp(steps), shape[dim] // parts).reshape((-1,) + (1,) * (len(shape) - 1 - dim))
    return loudness


def noise(key, extent, scale, most, cuts=(), kind=jnp.bfloat16):
    entries = scale * jax.random.normal(key, extent, jnp.float32)
    if cuts:
        entries = entries * levels(key, extent, cuts, -0.22, 0.18)
    return jnp.clip(entries, -most, most).astype(kind)


def setup_inputs(seed: int = 0) -> dict:
    seeds = jax.random.split(jax.random.key(seed), 12)
    held = noise(seeds[0], (N_SEGMENT, TOKENS, D), 1.0, 6.0, ((0, 4), (1, 32)))
    text = noise(seeds[1], (TOKENS, D), 1.0, 6.0, ((0, 32),))
    frames = noise(seeds[2], (VIS, VD), 1.0, 6.0, ((0, 32),))
    join = draw_join(jax.random.fold_in(seeds[11], 71), 0)
    ln_gain = jnp.clip(1.0 + 0.18 * jax.random.normal(seeds[4], (VD,), jnp.float32), 0.1, 1.9)
    w_proj = noise(seeds[5], (VD, D), VD ** -0.5, 0.1875, ((0, 2),))
    b_proj = noise(seeds[6], (D,), 0.5, 3.0, (), jnp.float32)
    norm_gain = jnp.clip(1.0 + 0.18 * jax.random.normal(seeds[7], (LAYERS, D), jnp.float32), 0.1, 1.9)
    w_qkv = noise(seeds[8], (LAYERS, D, QKV), D ** -0.5, 0.09375, ((1, 32), (2, 2)))
    b_qkv = draw_b_qkv(jax.random.fold_in(seeds[11], 71), 0)
    w_out = noise(seeds[10], (LAYERS, QH * HD, D), 0.25, 1.5, ((1, 2), (2, 32)))
    return {"held": held, "text": text, "frames": frames, "join": join, "ln_gain": ln_gain, "w_proj": w_proj, "b_proj": b_proj, "norm_gain": norm_gain, "w_qkv": w_qkv, "b_qkv": b_qkv, "w_out": w_out}


def vision_rows(text, frames, join, ln_gain, w_proj, b_proj):
    inputs = frames.astype(jnp.float32)
    center = lax.optimization_barrier(jnp.mean(inputs, axis=1, keepdims=True))
    spread = lax.optimization_barrier(jnp.mean((inputs - center) * (inputs - center), axis=1, keepdims=True))
    normed_in = ((inputs - center) * lax.rsqrt(spread + 1e-06) * ln_gain.astype(jnp.float32)).astype(jnp.bfloat16)
    projected = jnp.dot(normed_in, w_proj, preferred_element_type=jnp.float32) + b_proj.astype(jnp.float32)
    positions = jnp.arange(TOKENS, dtype=jnp.int32)[:, None]
    starts = join.astype(jnp.int32)[None, :]
    inside = (positions >= starts) & (positions < starts + FRAME)
    frame_base = (jnp.arange(FRAMES, dtype=jnp.int32) * FRAME)[None, :]
    source = lax.optimization_barrier(jnp.sum(jnp.where(inside, frame_base + positions - starts, 0), axis=1)).astype(jnp.int32)
    is_vision = jnp.any(inside, axis=1)
    taken = jnp.take(projected, source, axis=0)
    return jnp.where(is_vision[:, None], taken, text.astype(jnp.float32)).astype(jnp.bfloat16)

def attention_layer(hidden_in, gain, weight_qkv, bias_qkv, weight_out):
    inputs = hidden_in.astype(jnp.float32)
    normed = (inputs * lax.rsqrt(lax.optimization_barrier(jnp.mean(inputs * inputs, axis=1, keepdims=True)) + 1e-06) * gain.astype(jnp.float32)).astype(jnp.bfloat16)
    merged = (jnp.dot(normed, weight_qkv, preferred_element_type=jnp.float32) + bias_qkv.astype(jnp.float32)).astype(jnp.bfloat16)
    grouped = merged.reshape(TOKENS, KVH, GROUP + 2, HD)
    queries = grouped[:, :, :GROUP, :]
    keys = grouped[:, :, GROUP, :].astype(jnp.float32)
    values = grouped[:, :, GROUP + 1, :].astype(jnp.float32)
    block_len = math.gcd(TOKENS, 512)
    block_count = TOKENS // block_len
    query_blocks = queries.reshape(block_count, block_len, KVH, GROUP, HD)
    key_pos = jnp.arange(TOKENS, dtype=jnp.int32)

    def one_block(packed):
        block_index, block_query = packed
        query_pos = block_index.astype(jnp.int32) * block_len + jnp.arange(block_len, dtype=jnp.int32)
        scores = jnp.einsum('qkgd,tkd->kgqt', block_query.astype(jnp.float32), keys) * HD ** (-0.5)
        allowed = (key_pos[None, :] <= query_pos[:, None])[None, None]
        scores = jnp.where(allowed, scores, -1e+30)
        peak = lax.optimization_barrier(jnp.max(scores, axis=-1, keepdims=True))
        weights = jnp.where(allowed, jnp.exp(scores - peak), 0.0)
        total = lax.optimization_barrier(jnp.sum(weights, axis=-1))
        rounded = lax.optimization_barrier(weights.astype(jnp.bfloat16)).astype(jnp.float32)
        mixed = jnp.einsum('kgqt,tkd->qkgd', rounded, values) / jnp.transpose(total, (2, 0, 1))[..., None]
        return mixed.astype(jnp.bfloat16).reshape(block_len, KVH * GROUP * HD)
    attended = lax.map(one_block, (jnp.arange(block_count, dtype=jnp.int32), query_blocks))
    attended = attended.reshape(TOKENS, QH * HD)
    return (inputs + jnp.dot(attended, weight_out, preferred_element_type=jnp.float32)).astype(jnp.bfloat16)

def reference(held, text, frames, join, ln_gain, w_proj, b_proj, norm_gain, w_qkv, b_qkv, w_out):
    results = [vision_rows(text, frames, join, ln_gain, w_proj, b_proj)]
    for layer_id in range(LAYERS):
        results.append(attention_layer(held[layer_id], norm_gain[layer_id], w_qkv[layer_id], b_qkv[layer_id], w_out[layer_id]))
    return jnp.stack(results)
```

```python
from functools import partial

import jax
import jax.numpy as jnp
from jax import lax
from jax.sharding import PartitionSpec as P

HD = 128
GROUP = 7
FRAME = 64


def shifted(value, axis, by):
    devices = lax.axis_size(axis)
    pairs = [(i, i + by) for i in range(devices) if 0 <= i + by < devices]
    return lax.ppermute(value, axis, pairs)


def update_state(softmax_state, query_flat, query_pos, keys_in, values_in, offset):
    peak_old, total_old, accum_old = softmax_state
    key_pos = jnp.arange(keys_in.shape[0], dtype=jnp.int32)
    scores = jnp.dot(query_flat, keys_in.T, preferred_element_type=jnp.float32) * HD ** (-0.5)
    allowed = key_pos[None, :] <= query_pos[:, None]
    scores = jnp.where(allowed, scores, -1e30)
    peak_new = jnp.maximum(peak_old, jnp.max(scores, axis=1))
    weights = jnp.where(allowed, jnp.exp(scores - peak_new[:, None]), 0.0)
    total_new = jnp.sum(weights, axis=1)
    accum_new = jnp.dot(weights.astype(jnp.bfloat16), values_in, preferred_element_type=jnp.float32)
    return (peak_new, total_new, accum_new)


def keep_state(softmax_state):
    return softmax_state


def on_device(held, text, frames, join, ln_gain, w_proj, b_proj, norm_gain, w_qkv, b_qkv, w_out):
    segment_id = lax.axis_index("segment")
    ctx_id = lax.axis_index("ctx")
    tp_id = lax.axis_index("tp")
    hidden_in = shifted(held[0], "segment", 1)
    tok_rows = hidden_in.shape[0]
    half_rows = tok_rows // 2
    layer_id = jnp.maximum(segment_id - 1, 0)
    weight_qkv = lax.dynamic_index_in_dim(w_qkv, layer_id, 0, keepdims=False)
    bias_qkv = lax.dynamic_index_in_dim(b_qkv, layer_id, 0, keepdims=False)
    layer_gain = lax.dynamic_index_in_dim(norm_gain, layer_id, 0, keepdims=False)
    weight_out = lax.dynamic_index_in_dim(w_out, layer_id, 0, keepdims=False)
    inputs = hidden_in.astype(jnp.float32)
    normed = (
        inputs * lax.rsqrt(jnp.mean(inputs * inputs, axis=1, keepdims=True) + 1e-06) * layer_gain
    ).astype(jnp.bfloat16)
    merged = jnp.dot(
        normed,
        lax.all_gather(weight_qkv, "ctx", axis=0, tiled=True),
        preferred_element_type=jnp.float32,
    )
    merged = (merged + bias_qkv).astype(jnp.bfloat16)
    query_cols = GROUP * HD
    queries = merged[:, :query_cols]
    local_steps = jnp.arange(half_rows, dtype=jnp.int32)
    first_pos = ctx_id * tok_rows + local_steps
    second_q = queries[half_rows:]
    second_pos = ctx_id * tok_rows + half_rows + local_steps
    first_flat = queries[:half_rows].reshape(half_rows * GROUP, HD)
    second_flat = second_q.reshape(half_rows * GROUP, HD)
    first_qpos = jnp.repeat(first_pos, GROUP)
    second_qpos = jnp.repeat(second_pos, GROUP)
    flat_rows = half_rows * GROUP
    empty = (
        jnp.full((flat_rows,), -1e30, jnp.float32),
        jnp.zeros((flat_rows,), jnp.float32),
        jnp.zeros((flat_rows, HD), jnp.float32),
    )
    carried = (empty, empty)
    offset = jnp.int32(0)
    kv_in = lax.all_gather(merged[:, query_cols : query_cols + 2 * HD], "ctx", axis=0, tiled=True)
    keys_in = kv_in[:, :HD]
    values_in = kv_in[:, HD:]
    updated = []
    for softmax_state, query_flat, query_pos in (
        (carried[0], first_flat, first_qpos),
        (carried[1], second_flat, second_qpos),
    ):
        step_fn = partial(
            update_state,
            query_flat=query_flat,
            query_pos=query_pos,
            keys_in=keys_in,
            values_in=values_in,
            offset=offset,
        )
        updated.append(lax.cond(offset <= jnp.max(query_pos), step_fn, keep_state, softmax_state))

    def finish(softmax_state):
        return (
            (softmax_state[2] / softmax_state[1][:, None])
            .astype(jnp.bfloat16)
            .reshape(half_rows, GROUP * HD)
        )

    first_out = finish(updated[0])
    second_out = finish(updated[1])
    attended = jnp.concatenate([first_out, second_out], axis=0)
    partial_model = jnp.dot(
        attended,
        lax.all_gather(weight_out, "ctx", axis=1, tiled=True),
        preferred_element_type=jnp.float32,
    )
    positions = ctx_id * tok_rows + jnp.arange(tok_rows, dtype=jnp.int32)[:, None]
    starts = join[None, :]
    inside = (positions >= starts) & (positions < starts + FRAME)
    frame_base = (jnp.arange(join.shape[0], dtype=jnp.int32) * FRAME)[None, :]
    source = jnp.sum(jnp.where(inside, frame_base + positions - starts, 0), axis=1)
    is_vision = jnp.any(inside, axis=1)

    def vision_term():
        frame_in = frames.astype(jnp.float32)
        center = jnp.mean(frame_in, axis=1, keepdims=True)
        spread = jnp.mean((frame_in - center) * (frame_in - center), axis=1, keepdims=True)
        normed_frames = ((frame_in - center) * lax.rsqrt(spread + 1e-06) * ln_gain).astype(
            jnp.bfloat16
        )
        vis_width = w_proj.shape[0]
        normed_half = lax.dynamic_slice_in_dim(normed_frames, tp_id * vis_width, vis_width, 1)
        projected = jnp.dot(normed_half, w_proj, preferred_element_type=jnp.float32)
        return jnp.where(is_vision[:, None], jnp.take(projected, source, axis=0), 0.0)

    def model_term():
        return partial_model

    is_first = segment_id == 0
    section_term = lax.cond(is_first, vision_term, model_term)
    baseline = jnp.where(
        is_first, jnp.where(is_vision[:, None], b_proj[None, :], text.astype(jnp.float32)), inputs
    )
    own_term = section_term.astype(jnp.bfloat16)
    other_term = lax.ppermute(own_term, "tp", [(0, 1), (1, 0)])
    summed = own_term.astype(jnp.float32) + other_term.astype(jnp.float32)
    result = (baseline + summed).astype(jnp.bfloat16)
    return result[None]


def solution(mesh):
    return jax.shard_map(
        on_device,
        mesh=mesh,
        in_specs=(
            P("segment", "ctx", None),
            P("ctx", None),
            P("ctx", None),
            P("ctx"),
            P(),
            P("tp", None),
            P(),
            P(),
            P(None, "ctx", "tp"),
            P(None, "tp"),
            P(None, "tp", "ctx"),
        ),
        out_specs=P("segment", "ctx", None),
        check_vma=False,
    )
```

```python
import jax
import jax.numpy as jnp
from jax import lax
from jax.experimental import pallas as pl
from jax.experimental.pallas import tpu as pltpu
from jax.sharding import PartitionSpec as P

HD = 128
GROUP = 7
FRAME = 64
KEY_BLOCK = 512


def attention_kernel(ctx_ref, q_ref, k_ref, v_ref, o_ref, m_sc, l_sc, acc_sc):
    step_id = pl.program_id(0)
    rows = q_ref.shape[0]
    q_start = ctx_ref[0] * rows
    last_step = (q_start + rows - 1) // KEY_BLOCK

    @pl.when(step_id == 0)
    def _():
        m_sc[...] = jnp.full(m_sc.shape, -1e30, jnp.float32)
        l_sc[...] = jnp.zeros(l_sc.shape, jnp.float32)
        acc_sc[...] = jnp.zeros(acc_sc.shape, jnp.float32)

    def update(masked):
        keys = k_ref[...]
        values = v_ref[...]
        if masked:
            query_pos = q_start + lax.broadcasted_iota(jnp.int32, (rows, KEY_BLOCK), 0)
            key_pos = step_id * KEY_BLOCK + lax.broadcasted_iota(jnp.int32, (rows, KEY_BLOCK), 1)
            allowed = key_pos <= query_pos
        for head in range(GROUP):
            cols = slice(head * HD, (head + 1) * HD)
            scores = lax.dot_general(
                q_ref[:, cols], keys, (((1,), (1,)), ((), ())), preferred_element_type=jnp.float32
            ) * HD ** (-0.5)
            if masked:
                scores = jnp.where(allowed, scores, -1e30)
            peak_old = m_sc[head]
            peak_new = jnp.maximum(peak_old, jnp.max(scores, axis=1, keepdims=True))
            rescale = jnp.exp(peak_old - peak_new)
            weights = jnp.exp(scores - peak_new)
            if masked:
                weights = jnp.where(allowed, weights, 0.0)
            l_sc[head] = rescale * l_sc[head] + jnp.sum(weights, axis=1, keepdims=True)
            acc_sc[:, cols] = rescale * acc_sc[:, cols] + jnp.dot(
                weights.astype(jnp.bfloat16), values, preferred_element_type=jnp.float32
            )
            m_sc[head] = peak_new

    @pl.when((step_id + 1) * KEY_BLOCK - 1 <= q_start)
    def _():
        update(False)

    @pl.when(jnp.logical_and((step_id + 1) * KEY_BLOCK - 1 > q_start, step_id <= last_step))
    def _():
        update(True)

    @pl.when(step_id == pl.num_programs(0) - 1)
    def _():
        for head in range(GROUP):
            cols = slice(head * HD, (head + 1) * HD)
            o_ref[:, cols] = (acc_sc[:, cols] / l_sc[head]).astype(o_ref.dtype)


def causal_attention(ctx_id, merged, kv_in):
    rows = merged.shape[0]
    tokens = kv_in.shape[0]
    width = GROUP * HD

    def kv_map(col):
        def index(step_id, ctx_ref):
            last_step = (ctx_ref[0] * rows + rows - 1) // KEY_BLOCK
            return (jnp.minimum(step_id, last_step), col)
        return index

    flops = 4 * rows * GROUP * tokens * HD
    return pl.pallas_call(
        attention_kernel,
        out_shape=jax.ShapeDtypeStruct((rows, width), jnp.bfloat16),
        grid_spec=pltpu.PrefetchScalarGridSpec(
            num_scalar_prefetch=1,
            grid=(tokens // KEY_BLOCK,),
            in_specs=[
                pl.BlockSpec((rows, width), lambda step_id, ctx_ref: (0, 0)),
                pl.BlockSpec((KEY_BLOCK, HD), kv_map(0)),
                pl.BlockSpec((KEY_BLOCK, HD), kv_map(1)),
            ],
            out_specs=pl.BlockSpec((rows, width), lambda step_id, ctx_ref: (0, 0)),
            scratch_shapes=[
                pltpu.VMEM((GROUP, rows, 1), jnp.float32),
                pltpu.VMEM((GROUP, rows, 1), jnp.float32),
                pltpu.VMEM((rows, width), jnp.float32),
            ],
        ),
        compiler_params=pltpu.CompilerParams(dimension_semantics=("arbitrary",)),
        cost_estimate=pl.CostEstimate(
            flops=flops, transcendentals=rows * GROUP * tokens, bytes_accessed=kv_in.size * 2 + 4 * rows * width
        ),
    )(jnp.reshape(ctx_id, (1,)).astype(jnp.int32), merged, kv_in, kv_in)


def shifted(value, axis, by):
    devices = lax.axis_size(axis)
    pairs = [(i, i + by) for i in range(devices) if 0 <= i + by < devices]
    return lax.ppermute(value, axis, pairs)


def on_device(held, text, frames, join, ln_gain, w_proj, b_proj, norm_gain, w_qkv, b_qkv, w_out):
    segment_id = lax.axis_index("segment")
    ctx_id = lax.axis_index("ctx")
    tp_id = lax.axis_index("tp")
    hidden_in = shifted(held[0], "segment", 1)
    tok_rows = hidden_in.shape[0]
    layer_id = jnp.maximum(segment_id - 1, 0)
    weight_qkv = lax.dynamic_index_in_dim(w_qkv, layer_id, 0, keepdims=False)
    bias_qkv = lax.dynamic_index_in_dim(b_qkv, layer_id, 0, keepdims=False)
    layer_gain = lax.dynamic_index_in_dim(norm_gain, layer_id, 0, keepdims=False)
    weight_out = lax.dynamic_index_in_dim(w_out, layer_id, 0, keepdims=False)
    qkv_cols = weight_qkv.shape[1]
    packed = jnp.concatenate([weight_qkv, weight_out.T], axis=1)
    gathered = lax.all_gather(packed, "ctx", axis=0, tiled=True)
    weight_qkv_full = gathered[:, :qkv_cols]
    weight_out_cols = gathered[:, qkv_cols:]
    inputs = hidden_in.astype(jnp.float32)
    normed = (
        inputs * lax.rsqrt(jnp.mean(inputs * inputs, axis=1, keepdims=True) + 1e-06) * layer_gain
    ).astype(jnp.bfloat16)
    merged = jnp.dot(normed, weight_qkv_full, preferred_element_type=jnp.float32)
    merged = (merged + bias_qkv).astype(jnp.bfloat16)
    query_cols = GROUP * HD
    kv_in = lax.all_gather(merged[:, query_cols : query_cols + 2 * HD], "ctx", axis=0, tiled=True)
    attended = causal_attention(ctx_id, merged, kv_in)
    partial_model = lax.dot_general(
        attended, weight_out_cols, (((1,), (1,)), ((), ())), preferred_element_type=jnp.float32
    )
    positions = ctx_id * tok_rows + jnp.arange(tok_rows, dtype=jnp.int32)[:, None]
    starts = join[None, :]
    inside = (positions >= starts) & (positions < starts + FRAME)
    frame_base = (jnp.arange(join.shape[0], dtype=jnp.int32) * FRAME)[None, :]
    source = jnp.sum(jnp.where(inside, frame_base + positions - starts, 0), axis=1)
    is_vision = jnp.any(inside, axis=1)

    def vision_term():
        frame_in = frames.astype(jnp.float32)
        center = jnp.mean(frame_in, axis=1, keepdims=True)
        spread = jnp.mean((frame_in - center) * (frame_in - center), axis=1, keepdims=True)
        normed_frames = ((frame_in - center) * lax.rsqrt(spread + 1e-06) * ln_gain).astype(
            jnp.bfloat16
        )
        vis_width = w_proj.shape[0]
        normed_half = lax.dynamic_slice_in_dim(normed_frames, tp_id * vis_width, vis_width, 1)
        projected = jnp.dot(normed_half, w_proj, preferred_element_type=jnp.float32)
        return jnp.where(is_vision[:, None], jnp.take(projected, source, axis=0), 0.0)

    def model_term():
        return partial_model

    is_first = segment_id == 0
    section_term = lax.cond(is_first, vision_term, model_term)
    baseline = jnp.where(
        is_first, jnp.where(is_vision[:, None], b_proj[None, :], text.astype(jnp.float32)), inputs
    )
    own_term = section_term.astype(jnp.bfloat16)
    other_term = lax.ppermute(own_term, "tp", [(0, 1), (1, 0)])
    summed = own_term.astype(jnp.float32) + other_term.astype(jnp.float32)
    result = (baseline + summed).astype(jnp.bfloat16)
    return result[None]


def solution(mesh):
    return jax.shard_map(
        on_device,
        mesh=mesh,
        in_specs=(
            P("segment", "ctx", None),
            P("ctx", None),
            P("ctx", None),
            P("ctx"),
            P(),
            P("tp", None),
            P(),
            P(),
            P(None, "ctx", "tp"),
            P(None, "tp"),
            P(None, "tp", "ctx"),
        ),
        out_specs=P("segment", "ctx", None),
        check_vma=False,
    )
```

```python
import jax
import jax.numpy as jnp
from jax import lax
from jax.experimental import pallas as pl
from jax.experimental.pallas import tpu as pltpu
from jax.sharding import PartitionSpec as P

HD = 128
GROUP = 7
FRAME = 64
KEY_BLOCK = 2048
CHUNKS = 1


def attention_kernel(ctx_ref, q_ref, k_ref, v_ref, o_ref, m_sc, l_sc, acc_sc):
    step_id = pl.program_id(0)
    rows = q_ref.shape[0]
    q_start = ctx_ref[0]
    last_step = (q_start + rows - 1) // KEY_BLOCK

    @pl.when(step_id == 0)
    def _():
        m_sc[...] = jnp.full(m_sc.shape, -1e30, jnp.float32)
        l_sc[...] = jnp.zeros(l_sc.shape, jnp.float32)
        acc_sc[...] = jnp.zeros(acc_sc.shape, jnp.float32)

    def update(masked):
        keys = k_ref[...]
        values = v_ref[...]
        if masked:
            query_pos = q_start + lax.broadcasted_iota(jnp.int32, (rows, KEY_BLOCK), 0)
            key_pos = step_id * KEY_BLOCK + lax.broadcasted_iota(jnp.int32, (rows, KEY_BLOCK), 1)
            allowed = key_pos <= query_pos
        for head in range(GROUP):
            cols = slice(head * HD, (head + 1) * HD)
            scores = lax.dot_general(
                q_ref[:, cols], keys, (((1,), (1,)), ((), ())), preferred_element_type=jnp.float32
            ) * HD ** (-0.5)
            if masked:
                scores = jnp.where(allowed, scores, -1e30)
            peak_old = m_sc[head]
            peak_new = jnp.maximum(peak_old, jnp.max(scores, axis=1, keepdims=True))
            rescale = jnp.exp(peak_old - peak_new)
            weights = jnp.exp(scores - peak_new)
            if masked:
                weights = jnp.where(allowed, weights, 0.0)
            l_sc[head] = rescale * l_sc[head] + jnp.sum(weights, axis=1, keepdims=True)
            acc_sc[:, cols] = rescale * acc_sc[:, cols] + jnp.dot(
                weights.astype(jnp.bfloat16), values, preferred_element_type=jnp.float32
            )
            m_sc[head] = peak_new

    @pl.when((step_id + 1) * KEY_BLOCK - 1 <= q_start)
    def _():
        update(False)

    @pl.when(jnp.logical_and((step_id + 1) * KEY_BLOCK - 1 > q_start, step_id <= last_step))
    def _():
        update(True)

    @pl.when(step_id == pl.num_programs(0) - 1)
    def _():
        for head in range(GROUP):
            cols = slice(head * HD, (head + 1) * HD)
            o_ref[:, cols] = (acc_sc[:, cols] / l_sc[head]).astype(o_ref.dtype)


def causal_attention(q_start, merged, kv_in, chunk, rows):
    tokens = kv_in.shape[0]
    width = GROUP * HD

    def kv_map(col):
        def index(step_id, start_ref):
            last_step = (start_ref[0] + rows - 1) // KEY_BLOCK
            return (jnp.minimum(step_id, last_step), col)
        return index

    flops = 4 * rows * GROUP * tokens * HD
    return pl.pallas_call(
        attention_kernel,
        out_shape=jax.ShapeDtypeStruct((rows, width), jnp.bfloat16),
        grid_spec=pltpu.PrefetchScalarGridSpec(
            num_scalar_prefetch=1,
            grid=(tokens // KEY_BLOCK,),
            in_specs=[
                pl.BlockSpec((rows, width), lambda step_id, start_ref: (chunk, 0)),
                pl.BlockSpec((KEY_BLOCK, HD), kv_map(0)),
                pl.BlockSpec((KEY_BLOCK, HD), kv_map(1)),
            ],
            out_specs=pl.BlockSpec((rows, width), lambda step_id, start_ref: (0, 0)),
            scratch_shapes=[
                pltpu.VMEM((GROUP, rows, 1), jnp.float32),
                pltpu.VMEM((GROUP, rows, 1), jnp.float32),
                pltpu.VMEM((rows, width), jnp.float32),
            ],
        ),
        compiler_params=pltpu.CompilerParams(dimension_semantics=("arbitrary",)),
        cost_estimate=pl.CostEstimate(
            flops=flops, transcendentals=rows * GROUP * tokens, bytes_accessed=kv_in.size * 2 + 4 * rows * width
        ),
    )(jnp.reshape(q_start, (1,)).astype(jnp.int32), merged, kv_in, kv_in)


def shifted(value, axis, by):
    devices = lax.axis_size(axis)
    pairs = [(i, i + by) for i in range(devices) if 0 <= i + by < devices]
    return lax.ppermute(value, axis, pairs)


def on_device(held, text, frames, join, ln_gain, w_proj, b_proj, norm_gain, w_qkv, b_qkv, w_out):
    segment_id = lax.axis_index("segment")
    ctx_id = lax.axis_index("ctx")
    tp_id = lax.axis_index("tp")
    hidden_in = shifted(held[0], "segment", 1)
    tok_rows = hidden_in.shape[0]
    layer_id = jnp.maximum(segment_id - 1, 0)
    weight_qkv = lax.dynamic_index_in_dim(w_qkv, layer_id, 0, keepdims=False)
    bias_qkv = lax.dynamic_index_in_dim(b_qkv, layer_id, 0, keepdims=False)
    layer_gain = lax.dynamic_index_in_dim(norm_gain, layer_id, 0, keepdims=False)
    weight_out = lax.dynamic_index_in_dim(w_out, layer_id, 0, keepdims=False)
    qkv_cols = weight_qkv.shape[1]
    packed = jnp.concatenate([weight_qkv, weight_out.T], axis=1)
    gathered = lax.all_gather(packed, "ctx", axis=0, tiled=True)
    weight_qkv_full = gathered[:, :qkv_cols]
    weight_out_cols = gathered[:, qkv_cols:]
    inputs = hidden_in.astype(jnp.float32)
    normed = (
        inputs * lax.rsqrt(jnp.mean(inputs * inputs, axis=1, keepdims=True) + 1e-06) * layer_gain
    ).astype(jnp.bfloat16)
    merged = jnp.dot(normed, weight_qkv_full, preferred_element_type=jnp.float32)
    merged = (merged + bias_qkv).astype(jnp.bfloat16)
    query_cols = GROUP * HD
    kv_in = lax.all_gather(merged[:, query_cols : query_cols + 2 * HD], "ctx", axis=0, tiled=True)
    positions = ctx_id * tok_rows + jnp.arange(tok_rows, dtype=jnp.int32)[:, None]
    starts = join[None, :]
    inside = (positions >= starts) & (positions < starts + FRAME)
    frame_base = (jnp.arange(join.shape[0], dtype=jnp.int32) * FRAME)[None, :]
    source = jnp.sum(jnp.where(inside, frame_base + positions - starts, 0), axis=1)
    is_vision = jnp.any(inside, axis=1)

    def vision_term():
        frame_in = frames.astype(jnp.float32)
        center = jnp.mean(frame_in, axis=1, keepdims=True)
        spread = jnp.mean((frame_in - center) * (frame_in - center), axis=1, keepdims=True)
        normed_frames = ((frame_in - center) * lax.rsqrt(spread + 1e-06) * ln_gain).astype(
            jnp.bfloat16
        )
        vis_width = w_proj.shape[0]
        normed_half = lax.dynamic_slice_in_dim(normed_frames, tp_id * vis_width, vis_width, 1)
        projected = jnp.dot(normed_half, w_proj, preferred_element_type=jnp.float32)
        return jnp.where(is_vision[:, None], jnp.take(projected, source, axis=0), 0.0)

    is_first = segment_id == 0
    vision_rows = lax.cond(is_first, vision_term, lambda: jnp.zeros((tok_rows, w_proj.shape[1]), jnp.float32))
    chunk_rows = tok_rows // CHUNKS
    pieces = []
    own_term = None
    for chunk in range(CHUNKS):
        rows_here = slice(chunk * chunk_rows, (chunk + 1) * chunk_rows)
        if own_term is not None:
            own_term, merged = lax.optimization_barrier((own_term, merged))
            pieces[-1] = (pieces[-1][0], own_term)
        attended = causal_attention(
            ctx_id * tok_rows + chunk * chunk_rows, merged, kv_in, chunk, chunk_rows
        )
        partial_model = lax.dot_general(
            attended, weight_out_cols, (((1,), (1,)), ((), ())), preferred_element_type=jnp.float32
        )
        section_term = jnp.where(is_first, vision_rows[rows_here], partial_model)
        baseline = jnp.where(
            is_first,
            jnp.where(is_vision[rows_here, None], b_proj[None, :], text[rows_here].astype(jnp.float32)),
            inputs[rows_here],
        )
        own_term = section_term.astype(jnp.bfloat16)
        pieces.append((baseline, own_term))
    results = []
    for baseline, own_term in pieces:
        other_term = lax.ppermute(own_term, "tp", [(0, 1), (1, 0)])
        summed = own_term.astype(jnp.float32) + other_term.astype(jnp.float32)
        results.append((baseline + summed).astype(jnp.bfloat16))
    result = jnp.concatenate(results, axis=0)
    return result[None]


def solution(mesh):
    return jax.shard_map(
        on_device,
        mesh=mesh,
        in_specs=(
            P("segment", "ctx", None),
            P("ctx", None),
            P("ctx", None),
            P("ctx"),
            P(),
            P("tp", None),
            P(),
            P(),
            P(None, "ctx", "tp"),
            P(None, "tp"),
            P(None, "tp", "ctx"),
        ),
        out_specs=P("segment", "ctx", None),
        check_vma=False,
    )
```
